256 devices in a mesh: row: 16 (over x, y), ka: 16 (over z, core).
Axes of the slice: x: 4, y: 4, z: 8, core: 2. Of those that a mesh axis runs over, the one named last changes fastest.
Arguments:
- t2: bfloat16 [16, 4096, 128], P('row', 'ka'), may hold values from -6 to 6
- vtiles: bfloat16 [16, 16, 160, 128, 128], P('row', 'ka'), may hold values from -0.078125 to 0.078125
- need_cd: int32 [16, 16, 64], P(None, 'ka'), may hold values from 0 to 255, as said below
- tile_cd: int32 [16, 16, 160], P('row', 'ka'), may hold values from 0 to 63
- tile_ab: int32 [16, 16, 160], P('row', 'ka'), may hold values from 0 to 63
Outputs:
- ladder: bfloat16 [1024, 16, 128], P(('row', 'ka'))
The draws below stay inside these ranges and needn't reach their ends.
Inputs may be any that keep to these rules, and one draw needn't show every extreme that they name: `need_cd`: the 64 entries of one block's list are all different.
All inputs are finite; a program needn't handle non-finite values.
Results may differ from the reference program's by a relative error of at most 0.0015.
Values may be sent and summed in bfloat16 or wider, within the bound.
No kernel may reach another device: no remote copies, remote signals or barrier semaphores. Data moves between devices by JAX's collectives and lax.ppermute only.
A program may use at most 64 MiB of HBM per device.

```python
import jax
import jax.numpy as jnp
from jax import lax

PAIRS = 16
TILE = 128
CD_DEV = 256
AB_DEV = 64
QCAP = 64
SLOTS = 160
NCD = 4096
N_ROW = 16
N_KA = 16


def draw_need_cd(key, part):
    subkeys = jax.random.split(key, N_ROW * N_KA)

    def chosen(subkey):
        return jax.random.permutation(subkey, CD_DEV)[:QCAP]
    listed = jax.vmap(chosen)(subkeys)
    return listed.reshape(N_ROW, N_KA, QCAP).astype(jnp.int32)


def set_ends(entries, rng, least, largest):
    extent = entries.shape
    place = [jax.random.randint(jax.random.fold_in(rng, axis), (), 0, extent[axis]) for axis in range(len(extent))]
    entries = entries.at[tuple(place)].set(least)
    longest = extent.index(max(extent))
    place[longest] = (place[longest] + 1) % extent[longest]
    return entries.at[tuple(place)].set(largest)


def block_scale(own_key, extent, cuts, smallest, top_value):
    gain, own = 1.0, jax.random.fold_in(own_key, 6)
    for axis_at, blocks in cuts:
        heights = jnp.exp(jax.random.uniform(jax.random.fold_in(own, axis_at), (blocks,), jnp.float32, smallest / len(cuts), top_value / len(cuts)))
        gain = gain * jnp.repeat(heights, extent[axis_at] // blocks).reshape([-1 if axis == axis_at else 1 for axis in range(len(extent))])
    return gain


def centred(stream_key, extent, spread, bound, cuts=(), kind=jnp.bfloat16):
    loudness = block_scale(stream_key, extent, cuts, -0.22, 0.18) if cuts else 1.0
    drawn = jax.random.normal(stream_key, extent, jnp.float32) * spread * loudness
    return jnp.minimum(jnp.maximum(drawn, -bound), bound).astype(kind)


def setup_inputs(seed: int = 0) -> dict:
    key_list = jax.random.split(jax.random.key(seed), 6)
    return {
        "t2": centred(key_list[0], (PAIRS, NCD, TILE), 1.0, 6.0, ((0, 16), (1, 16))),
        "vtiles": centred(key_list[1], (N_ROW, N_KA, SLOTS, TILE, TILE), (TILE * max(1, SLOTS * N_KA // AB_DEV)) ** -0.5, 0.078125, ((0, 16), (1, 16))),
        "need_cd": draw_need_cd(jax.random.fold_in(key_list[5], 71), 0),
        "tile_cd": set_ends(jax.random.randint(key_list[3], (N_ROW, N_KA, SLOTS), 0, QCAP), jax.random.fold_in(key_list[3], 1), 0, QCAP - 1).astype(jnp.int32),
        "tile_ab": set_ends(jax.random.randint(key_list[4], (N_ROW, N_KA, SLOTS), 0, AB_DEV), jax.random.fold_in(key_list[4], 1), 0, AB_DEV - 1).astype(jnp.int32),
    }


def reference(t2, vtiles, need_cd, tile_cd, tile_ab):
    accumulated = jnp.zeros((AB_DEV * N_ROW, PAIRS, TILE), jnp.float32)
    offsets = (jnp.arange(N_KA, dtype=jnp.int32) * CD_DEV)[:, None]

    def advance(carried, sliced):
        blocks, wanted, slot_cd, slot_ab, row_index = sliced
        columns = jnp.take_along_axis(wanted, slot_cd, axis=1).astype(jnp.int32) + offsets
        picked = t2[:, columns, :].astype(jnp.float32)
        products = jnp.einsum("pkst,kstu->kspu", picked, blocks.astype(jnp.float32))
        targets = (row_index * AB_DEV + slot_ab).astype(jnp.int32)
        carried = carried.at[targets.reshape(-1)].add(products.reshape(-1, PAIRS, TILE))
        return carried, None

    sliced = (vtiles, need_cd, tile_cd, tile_ab, jnp.arange(N_ROW, dtype=jnp.int32))
    accumulated, _ = lax.scan(advance, accumulated, sliced)
    return accumulated.astype(jnp.bfloat16)
```

```python
import jax
import jax.numpy as jnp
from jax import lax
from jax.sharding import PartitionSpec as P

AB_DEV = 64


def gather_oh(t2, need_cd):
    lists = need_cd[:, 0, :]
    send = jnp.take(t2[0], lists, axis=0)
    return lax.all_to_all(send, "row", 0, 0, tiled=True)


def gather_pp(t2, need_cd):
    n = lax.axis_size("row")
    me = lax.axis_index("row")
    lists = need_cd[:, 0, :]
    own = lax.dynamic_index_in_dim(lists, me, 0, keepdims=False)
    parts = [None] * n
    parts[0] = jnp.take(t2[0], own, axis=0)
    for j in range(1, n):
        dest = (me + j) % n
        rows = lax.dynamic_index_in_dim(lists, dest, 0, keepdims=False)
        got = lax.ppermute(jnp.take(t2[0], rows, axis=0), "row", [(i, (i + j) % n) for i in range(n)])
        parts[j] = got
    stacked = jnp.stack(parts)
    src = (me - jnp.arange(n)) % n
    order = jnp.argsort(src)
    return jnp.take(stacked, order, axis=0)


def gather_ag(t2, need_cd):
    own = lax.dynamic_index_in_dim(need_cd[:, 0, :], lax.axis_index("row"), 0, keepdims=False)
    whole = lax.all_gather(t2, "row", axis=0, tiled=True)
    return jnp.take(whole, own, axis=1)


def reduce_rs(summed):
    return lax.psum_scatter(summed, "ka", scatter_dimension=0, tiled=True)


def reduce_h(summed):
    n = (lax.axis_size("z") * lax.axis_size("c"))
    s = summed.reshape(n, summed.shape[0] // n, *summed.shape[1:])
    got = lax.all_to_all(s, "ka", 0, 0, tiled=True)
    return got.sum(axis=0)


def reduce_pp(summed):
    n = (lax.axis_size("z") * lax.axis_size("c"))
    me = lax.axis_index("ka")
    share = summed.shape[0] // n
    s = summed.reshape(n, share, *summed.shape[1:])
    total = lax.dynamic_index_in_dim(s, me, 0, keepdims=False)
    for j in range(1, n):
        dest = (me + j) % n
        part = lax.dynamic_index_in_dim(s, dest, 0, keepdims=False)
        total = total + lax.ppermute(part, "ka", [(i, (i + j) % n) for i in range(n)])
    return total


def reduce_h(summed):
    nz = lax.axis_size("z")
    nc = lax.axis_size("c")
    share = summed.shape[0] // (nz * nc)
    s = summed.reshape(nz, nc, share, *summed.shape[1:])
    got = lax.all_to_all(s, "c", 1, 1, tiled=True)
    s = got.sum(axis=1)
    got = lax.all_to_all(s, "z", 0, 0, tiled=True)
    return got.sum(axis=0)


def gather_oh(t2, need_cd):
    lists = need_cd[:, 0, :]
    n_rows = t2.shape[1]
    onehot = (lists.reshape(-1)[:, None] == lax.iota(jnp.int32, n_rows)[None, :]).astype(t2.dtype)
    send = jnp.dot(onehot, t2[0], preferred_element_type=jnp.float32).astype(t2.dtype)
    send = send.reshape(lists.shape[0], lists.shape[1], t2.shape[2])
    return lax.all_to_all(send, "row", 0, 0, tiled=True)


def on_device(t2, vtiles, need_cd, tile_cd, tile_ab):
    pairs_all = t2.shape[0] * lax.axis_size("row")
    tile_edge = t2.shape[2]
    slot_cd = tile_cd[0, 0]
    slot_ab = tile_ab[0, 0]
    blocks = vtiles[0, 0]
    slot_count = slot_cd.shape[0]
    mine = gather_oh(t2, need_cd)
    picked = jnp.take(mine, slot_cd, axis=1)
    products = jnp.einsum("pst,stu->spu", picked, blocks, preferred_element_type=jnp.float32)
    products = products.reshape(slot_count, pairs_all * tile_edge)
    upper_part = lax.optimization_barrier(products.astype(jnp.bfloat16))
    lower_part = (products - upper_part.astype(jnp.float32)).astype(jnp.bfloat16)
    share = AB_DEV // (lax.axis_size("z") * lax.axis_size("c"))
    wanted_rows = lax.iota(jnp.int32, share * (lax.axis_size("z") * lax.axis_size("c")))
    onehot = (slot_ab[None, :] == wanted_rows[:, None]).astype(jnp.bfloat16)
    summed = jnp.dot(onehot, upper_part, preferred_element_type=jnp.float32)
    summed = summed + jnp.dot(onehot, lower_part, preferred_element_type=jnp.float32)
    reduced = reduce_h(summed.reshape(share * (lax.axis_size("z") * lax.axis_size("c")), pairs_all, tile_edge))
    return reduced.astype(jnp.bfloat16)


def solution(mesh):
    from jax.sharding import Mesh
    devs = mesh.devices
    n_ka = devs.shape[1]
    fine = Mesh(devs.reshape(devs.shape[0], n_ka // 2, 2), ("row", "z", "c"))
    return jax.shard_map(
        on_device,
        mesh=fine,
        in_specs=(
            P("row", ("z", "c"), None),
            P("row", ("z", "c"), None, None, None),
            P(None, ("z", "c"), None),
            P("row", ("z", "c"), None),
            P("row", ("z", "c"), None),
        ),
        out_specs=P(("row", "z", "c"), None, None),
        check_vma=False,
    )
```

```python
import jax
import jax.numpy as jnp
from jax import lax
from jax.sharding import PartitionSpec as P

AB_DEV = 64


def gather_oh(t2, need_cd):
    lists = need_cd[:, 0, :]
    send = jnp.take(t2[0], lists, axis=0)
    return lax.all_to_all(send, "row", 0, 0, tiled=True)


def gather_pp(t2, need_cd):
    n = lax.axis_size("row")
    me = lax.axis_index("row")
    lists = need_cd[:, 0, :]
    own = lax.dynamic_index_in_dim(lists, me, 0, keepdims=False)
    parts = [None] * n
    parts[0] = jnp.take(t2[0], own, axis=0)
    for j in range(1, n):
        dest = (me + j) % n
        rows = lax.dynamic_index_in_dim(lists, dest, 0, keepdims=False)
        got = lax.ppermute(jnp.take(t2[0], rows, axis=0), "row", [(i, (i + j) % n) for i in range(n)])
        parts[j] = got
    stacked = jnp.stack(parts)
    src = (me - jnp.arange(n)) % n
    order = jnp.argsort(src)
    return jnp.take(stacked, order, axis=0)


def gather_ag(t2, need_cd):
    own = lax.dynamic_index_in_dim(need_cd[:, 0, :], lax.axis_index("row"), 0, keepdims=False)
    whole = lax.all_gather(t2, "row", axis=0, tiled=True)
    return jnp.take(whole, own, axis=1)


def reduce_rs(summed):
    return lax.psum_scatter(summed, "ka", scatter_dimension=0, tiled=True)


def reduce_h(summed):
    n = (lax.axis_size("z") * lax.axis_size("c"))
    s = summed.reshape(n, summed.shape[0] // n, *summed.shape[1:])
    got = lax.all_to_all(s, "ka", 0, 0, tiled=True)
    return got.sum(axis=0)


def reduce_pp(summed):
    n = (lax.axis_size("z") * lax.axis_size("c"))
    me = lax.axis_index("ka")
    share = summed.shape[0] // n
    s = summed.reshape(n, share, *summed.shape[1:])
    total = lax.dynamic_index_in_dim(s, me, 0, keepdims=False)
    for j in range(1, n):
        dest = (me + j) % n
        part = lax.dynamic_index_in_dim(s, dest, 0, keepdims=False)
        total = total + lax.ppermute(part, "ka", [(i, (i + j) % n) for i in range(n)])
    return total


def reduce_h(summed):
    nz = lax.axis_size("z")
    nc = lax.axis_size("c")
    share = summed.shape[0] // (nz * nc)
    s = summed.reshape(nz, nc, share, *summed.shape[1:])
    got = lax.all_to_all(s, "c", 1, 1, tiled=True)
    s = got.sum(axis=1)
    got = lax.all_to_all(s, "z", 0, 0, tiled=True)
    return got.sum(axis=0)


def gather_oh(t2, need_cd):
    n_rows = t2.shape[1]
    onehot = (need_cd[..., None] == lax.iota(jnp.int32, n_rows)).astype(t2.dtype)
    send = jnp.einsum("dkqc,kct->dqt", onehot, t2, preferred_element_type=jnp.float32).astype(t2.dtype)
    return lax.all_to_all(send, "row", 0, 0, tiled=True)


def on_device(t2, vtiles, need_cd, tile_cd, tile_ab):
    pairs_all = t2.shape[0] * lax.axis_size("row")
    tile_edge = t2.shape[2]
    slot_cd = tile_cd[0, 0]
    slot_ab = tile_ab[0, 0]
    blocks = vtiles[0, 0]
    slot_count = slot_cd.shape[0]
    mine = gather_oh(t2, need_cd)
    picked = jnp.take(mine, slot_cd, axis=1)
    products = jnp.einsum("pst,stu->spu", picked, blocks, preferred_element_type=jnp.float32)
    products = products.reshape(slot_count, pairs_all * tile_edge)
    upper_part = lax.optimization_barrier(products.astype(jnp.bfloat16))
    lower_part = (products - upper_part.astype(jnp.float32)).astype(jnp.bfloat16)
    share = AB_DEV // (lax.axis_size("z") * lax.axis_size("c"))
    wanted_rows = lax.iota(jnp.int32, share * (lax.axis_size("z") * lax.axis_size("c")))
    onehot = (slot_ab[None, :] == wanted_rows[:, None]).astype(jnp.bfloat16)
    summed = jnp.dot(onehot, upper_part, preferred_element_type=jnp.float32)
    summed = summed + jnp.dot(onehot, lower_part, preferred_element_type=jnp.float32)
    reduced = reduce_h(summed.reshape(share * (lax.axis_size("z") * lax.axis_size("c")), pairs_all, tile_edge))
    return reduced.astype(jnp.bfloat16)


def solution(mesh):
    from jax.sharding import Mesh
    devs = mesh.devices
    n_ka = devs.shape[1]
    fine = Mesh(devs.reshape(devs.shape[0], n_ka // 2, 2), ("row", "z", "c"))
    return jax.shard_map(
        on_device,
        mesh=fine,
        in_specs=(
            P("row", ("z", "c"), None),
            P("row", ("z", "c"), None, None, None),
            P(None, ("z", "c"), None),
            P("row", ("z", "c"), None),
            P("row", ("z", "c"), None),
        ),
        out_specs=P(("row", "z", "c"), None, None),
        check_vma=False,
    )
```

```python
import jax
import jax.numpy as jnp
from jax import lax
from jax.sharding import PartitionSpec as P

AB_DEV = 64


def gather_oh(t2, need_cd):
    lists = need_cd[:, 0, :]
    send = jnp.take(t2[0], lists, axis=0)
    return lax.all_to_all(send, "row", 0, 0, tiled=True)


def gather_pp(t2, need_cd):
    n = lax.axis_size("row")
    me = lax.axis_index("row")
    lists = need_cd[:, 0, :]
    own = lax.dynamic_index_in_dim(lists, me, 0, keepdims=False)
    parts = [None] * n
    parts[0] = jnp.take(t2[0], own, axis=0)
    for j in range(1, n):
        dest = (me + j) % n
        rows = lax.dynamic_index_in_dim(lists, dest, 0, keepdims=False)
        got = lax.ppermute(jnp.take(t2[0], rows, axis=0), "row", [(i, (i + j) % n) for i in range(n)])
        parts[j] = got
    stacked = jnp.stack(parts)
    src = (me - jnp.arange(n)) % n
    order = jnp.argsort(src)
    return jnp.take(stacked, order, axis=0)


def gather_ag(t2, need_cd):
    own = lax.dynamic_index_in_dim(need_cd[:, 0, :], lax.axis_index("row"), 0, keepdims=False)
    whole = lax.all_gather(t2, "row", axis=0, tiled=True)
    return jnp.take(whole, own, axis=1)


def reduce_rs(summed):
    return lax.psum_scatter(summed, "ka", scatter_dimension=0, tiled=True)


def reduce_h(summed):
    n = (lax.axis_size("z") * lax.axis_size("c"))
    s = summed.reshape(n, summed.shape[0] // n, *summed.shape[1:])
    got = lax.all_to_all(s, "ka", 0, 0, tiled=True)
    return got.sum(axis=0)


def reduce_pp(summed):
    n = (lax.axis_size("z") * lax.axis_size("c"))
    me = lax.axis_index("ka")
    share = summed.shape[0] // n
    s = summed.reshape(n, share, *summed.shape[1:])
    total = lax.dynamic_index_in_dim(s, me, 0, keepdims=False)
    for j in range(1, n):
        dest = (me + j) % n
        part = lax.dynamic_index_in_dim(s, dest, 0, keepdims=False)
        total = total + lax.ppermute(part, "ka", [(i, (i + j) % n) for i in range(n)])
    return total


def reduce_h(summed):
    nz = lax.axis_size("z")
    nc = lax.axis_size("c")
    share = summed.shape[0] // (nz * nc)
    s = summed.reshape(nz, nc, share, *summed.shape[1:])
    got = lax.all_to_all(s, "c", 1, 1, tiled=True)
    s = got.sum(axis=1)
    got = lax.all_to_all(s, "z", 0, 0, tiled=True)
    return got.sum(axis=0)


def gather_oh(t2, need_cd):
    n_rows = t2.shape[1]
    onehot = (need_cd[..., None] == lax.iota(jnp.int32, n_rows)).astype(t2.dtype)
    send = jnp.einsum("dkqc,kct->dqt", onehot, t2, preferred_element_type=jnp.float32).astype(t2.dtype)
    return lax.all_to_all(send, "row", 0, 0, tiled=True)


def on_device(t2, vtiles, need_cd, tile_cd, tile_ab):
    pairs_all = t2.shape[0] * lax.axis_size("row")
    tile_edge = t2.shape[2]
    nz, nc = lax.axis_size("z"), lax.axis_size("c")
    share = AB_DEV // (nz * nc)
    slot_cd = tile_cd[0, 0]
    slot_ab = tile_ab[0, 0]
    blocks = vtiles[0, 0]
    slot_count = slot_cd.shape[0]
    mine = gather_oh(t2, need_cd)
    picked = jnp.take(mine, slot_cd, axis=1)
    products = jnp.einsum("pst,stu->spu", picked, blocks, preferred_element_type=jnp.float32)
    products = products.reshape(slot_count, pairs_all * tile_edge)
    owner = slot_ab // share
    placed = (owner % nc) * (nz * share) + (owner // nc) * share + slot_ab % share
    upper_part = lax.optimization_barrier(products.astype(jnp.bfloat16))
    lower_part = (products - upper_part.astype(jnp.float32)).astype(jnp.bfloat16)
    onehot = (placed[None, :] == lax.iota(jnp.int32, AB_DEV)[:, None]).astype(jnp.bfloat16)
    summed = jnp.dot(onehot, upper_part, preferred_element_type=jnp.float32)
    summed = summed + jnp.dot(onehot, lower_part, preferred_element_type=jnp.float32)
    s = summed.reshape(nc, nz, share, pairs_all, tile_edge)
    me = lax.axis_index("c")
    own = lax.dynamic_index_in_dim(s, me, 0, keepdims=False)
    other = lax.dynamic_index_in_dim(s, 1 - me, 0, keepdims=False)
    s = own + lax.ppermute(other, "c", [(0, 1), (1, 0)])
    s = lax.all_to_all(s, "z", 0, 0, tiled=True).sum(axis=0)
    return s.astype(jnp.bfloat16)


def solution(mesh):
    from jax.sharding import Mesh
    devs = mesh.devices
    n_ka = devs.shape[1]
    fine = Mesh(devs.reshape(devs.shape[0], n_ka // 2, 2), ("row", "z", "c"))
    return jax.shard_map(
        on_device,
        mesh=fine,
        in_specs=(
            P("row", ("z", "c"), None),
            P("row", ("z", "c"), None, None, None),
            P(None, ("z", "c"), None),
            P("row", ("z", "c"), None),
            P("row", ("z", "c"), None),
        ),
        out_specs=P(("row", "z", "c"), None, None),
        check_vma=False,
    )
```

```python
import functools

import jax
import jax.numpy as jnp
from jax import lax
from jax.experimental import pallas as pl
from jax.experimental.pallas import tpu as pltpu
from jax.sharding import Mesh
from jax.sharding import PartitionSpec as P

AB_DEV = 64


def gather_rows(t2, need_cd):
    n_rows = t2.shape[1]
    onehot = (need_cd[..., None] == lax.iota(jnp.int32, n_rows)).astype(t2.dtype)
    send = jnp.einsum("dkqc,kct->dqt", onehot, t2, preferred_element_type=jnp.float32).astype(t2.dtype)
    return lax.all_to_all(send, "row", 0, 0, tiled=True)


def reduce_rows(summed, nz, nc, share, pairs_all, tile_edge):
    s = summed.reshape(nc, nz, share, pairs_all, tile_edge)
    me = lax.axis_index("c")
    own = lax.dynamic_index_in_dim(s, me, 0, keepdims=False)
    other = lax.dynamic_index_in_dim(s, 1 - me, 0, keepdims=False)
    s = own + lax.ppermute(other, "c", [(0, 1), (1, 0)])
    s = lax.all_to_all(s, "z", 0, 0, tiled=True).sum(axis=0)
    return s.astype(jnp.bfloat16)


def on_device(t2, vtiles, need_cd, tile_cd, tile_ab):
    pairs_all = t2.shape[0] * lax.axis_size("row")
    tile_edge = t2.shape[2]
    nz, nc = lax.axis_size("z"), lax.axis_size("c")
    share = AB_DEV // (nz * nc)
    slot_cd = tile_cd[0, 0]
    slot_ab = tile_ab[0, 0]
    blocks = vtiles[0, 0]
    slot_count = slot_cd.shape[0]
    mine = gather_rows(t2, need_cd)
    picked = jnp.take(mine, slot_cd, axis=1)
    products = jnp.einsum("pst,stu->spu", picked, blocks, preferred_element_type=jnp.float32)
    products = products.reshape(slot_count, pairs_all * tile_edge)
    owner = slot_ab // share
    placed = (owner % nc) * (nz * share) + (owner // nc) * share + slot_ab % share
    upper_part = lax.optimization_barrier(products.astype(jnp.bfloat16))
    lower_part = (products - upper_part.astype(jnp.float32)).astype(jnp.bfloat16)
    onehot = (placed[None, :] == lax.iota(jnp.int32, AB_DEV)[:, None]).astype(jnp.bfloat16)
    summed = jnp.dot(onehot, upper_part, preferred_element_type=jnp.float32)
    summed = summed + jnp.dot(onehot, lower_part, preferred_element_type=jnp.float32)
    return reduce_rows(summed, nz, nc, share, pairs_all, tile_edge)


def solution(mesh):
    devs = mesh.devices
    n_ka = devs.shape[1]
    fine = Mesh(devs.reshape(devs.shape[0], n_ka // 2, 2), ("row", "z", "c"))
    cols = ("z", "c")
    return jax.shard_map(
        on_device,
        mesh=fine,
        in_specs=(
            P("row", cols, None),
            P("row", cols, None, None, None),
            P(None, cols, None),
            P("row", cols, None),
            P("row", cols, None),
        ),
        out_specs=P(("row", "z", "c"), None, None),
        check_vma=False,
    )
```

```python
import functools

import jax
import jax.numpy as jnp
from jax import lax
from jax.experimental import pallas as pl
from jax.experimental.pallas import tpu as pltpu
from jax.sharding import Mesh
from jax.sharding import PartitionSpec as P

AB_DEV = 64


def gather_rows(t2, need_cd):
    n_rows = t2.shape[1]
    onehot = (need_cd[..., None] == lax.iota(jnp.int32, n_rows)).astype(t2.dtype)
    send = jnp.einsum("dkqc,kct->dqt", onehot, t2, preferred_element_type=jnp.float32).astype(t2.dtype)
    return lax.all_to_all(send, "row", 0, 0, tiled=True)


def reduce_rows(summed, nz, nc, share, pairs_all, tile_edge):
    s = summed.reshape(nc, nz, share, pairs_all, tile_edge)
    me = lax.axis_index("c")
    own = lax.dynamic_index_in_dim(s, me, 0, keepdims=False)
    other = lax.dynamic_index_in_dim(s, 1 - me, 0, keepdims=False)
    s = own + lax.ppermute(other, "c", [(0, 1), (1, 0)])
    mz = lax.axis_index("z")
    total = lax.dynamic_index_in_dim(s, mz, 0, keepdims=False)
    for j in range(1, nz):
        part = lax.dynamic_index_in_dim(s, (mz + j) % nz, 0, keepdims=False)
        total = total + lax.ppermute(part, "z", [(i, (i + j) % nz) for i in range(nz)])
    s = total
    return s.astype(jnp.bfloat16)


def on_device(t2, vtiles, need_cd, tile_cd, tile_ab):
    pairs_all = t2.shape[0] * lax.axis_size("row")
    tile_edge = t2.shape[2]
    nz, nc = lax.axis_size("z"), lax.axis_size("c")
    share = AB_DEV // (nz * nc)
    slot_cd = tile_cd[0, 0]
    slot_ab = tile_ab[0, 0]
    blocks = vtiles[0, 0]
    slot_count = slot_cd.shape[0]
    mine = gather_rows(t2, need_cd)
    picked = jnp.take(mine, slot_cd, axis=1)
    products = jnp.einsum("pst,stu->spu", picked, blocks, preferred_element_type=jnp.float32)
    products = products.reshape(slot_count, pairs_all * tile_edge)
    owner = slot_ab // share
    placed = (owner % nc) * (nz * share) + (owner // nc) * share + slot_ab % share
    upper_part = lax.optimization_barrier(products.astype(jnp.bfloat16))
    lower_part = (products - upper_part.astype(jnp.float32)).astype(jnp.bfloat16)
    onehot = (placed[None, :] == lax.iota(jnp.int32, AB_DEV)[:, None]).astype(jnp.bfloat16)
    summed = jnp.dot(onehot, upper_part, preferred_element_type=jnp.float32)
    summed = summed + jnp.dot(onehot, lower_part, preferred_element_type=jnp.float32)
    return reduce_rows(summed, nz, nc, share, pairs_all, tile_edge)


def solution(mesh):
    devs = mesh.devices
    n_ka = devs.shape[1]
    fine = Mesh(devs.reshape(devs.shape[0], n_ka // 2, 2), ("row", "z", "c"))
    cols = ("z", "c")
    return jax.shard_map(
        on_device,
        mesh=fine,
        in_specs=(
            P("row", cols, None),
            P("row", cols, None, None, None),
            P(None, cols, None),
            P("row", cols, None),
            P("row", cols, None),
        ),
        out_specs=P(("row", "z", "c"), None, None),
        check_vma=False,
    )
```

```python
import functools

import jax
import jax.numpy as jnp
from jax import lax
from jax.experimental import pallas as pl
from jax.experimental.pallas import tpu as pltpu
from jax.sharding import Mesh
from jax.sharding import PartitionSpec as P

AB_DEV = 64


def gather_rows(t2, need_cd):
    n_rows = t2.shape[1]
    onehot = (need_cd[..., None] == lax.iota(jnp.int32, n_rows)).astype(t2.dtype)
    send = jnp.einsum("dkqc,kct->dqt", onehot, t2, preferred_element_type=jnp.float32).astype(t2.dtype)
    return lax.all_to_all(send, "row", 0, 0, tiled=True)


def reduce_rows(summed, nz, nc, share, pairs_all, tile_edge):
    s = summed.reshape(nc, nz, share, pairs_all, tile_edge)
    me = lax.axis_index("c")
    own = lax.dynamic_index_in_dim(s, me, 0, keepdims=False)
    other = lax.dynamic_index_in_dim(s, 1 - me, 0, keepdims=False)
    s = own + lax.ppermute(other, "c", [(0, 1), (1, 0)])
    mz = lax.axis_index("z")
    total = lax.dynamic_index_in_dim(s, mz, 0, keepdims=False)
    for j in range(1, nz):
        part = lax.dynamic_index_in_dim(s, (mz + j) % nz, 0, keepdims=False)
        total = total + lax.ppermute(part, "z", [(i, (i + j) % nz) for i in range(nz)])
    s = total
    return s.astype(jnp.bfloat16)


def on_device(t2, vtiles, need_cd, tile_cd, tile_ab):
    pairs_all = t2.shape[0] * lax.axis_size("row")
    tile_edge = t2.shape[2]
    nz, nc = lax.axis_size("z"), lax.axis_size("c")
    share = AB_DEV // (nz * nc)
    slot_cd = tile_cd[0, 0]
    slot_ab = tile_ab[0, 0]
    blocks = vtiles[0, 0]
    slot_count = slot_cd.shape[0]
    mine = gather_rows(t2, need_cd)
    picked = jnp.take(mine, slot_cd, axis=1)
    products = jnp.einsum("pst,stu->spu", picked, blocks, preferred_element_type=jnp.float32)
    products = products.reshape(slot_count, pairs_all * tile_edge)
    owner = slot_ab // share
    placed = (owner % nc) * (nz * share) + (owner // nc) * share + slot_ab % share
    upper_part = lax.optimization_barrier(products.astype(jnp.bfloat16))
    lower_part = (products - upper_part.astype(jnp.float32)).astype(jnp.bfloat16)
    me_c = lax.axis_index("c")
    half = nz * share
    rows_other = (1 - me_c) * half + lax.iota(jnp.int32, half)
    rows_own = me_c * half + lax.iota(jnp.int32, half)

    def scatter(rows):
        onehot = (placed[None, :] == rows[:, None]).astype(jnp.bfloat16)
        total = jnp.dot(onehot, upper_part, preferred_element_type=jnp.float32)
        return total + jnp.dot(onehot, lower_part, preferred_element_type=jnp.float32)

    other = scatter(rows_other).reshape(nz, share, pairs_all, tile_edge)
    moved = lax.ppermute(other, "c", [(0, 1), (1, 0)])
    s = scatter(rows_own).reshape(nz, share, pairs_all, tile_edge) + moved
    mz = lax.axis_index("z")
    total = lax.dynamic_index_in_dim(s, mz, 0, keepdims=False)
    for j in range(1, nz):
        part = lax.dynamic_index_in_dim(s, (mz + j) % nz, 0, keepdims=False)
        total = total + lax.ppermute(part, "z", [(i, (i + j) % nz) for i in range(nz)])
    return total.astype(jnp.bfloat16)


def solution(mesh):
    devs = mesh.devices
    n_ka = devs.shape[1]
    fine = Mesh(devs.reshape(devs.shape[0], n_ka // 2, 2), ("row", "z", "c"))
    cols = ("z", "c")
    return jax.shard_map(
        on_device,
        mesh=fine,
        in_specs=(
            P("row", cols, None),
            P("row", cols, None, None, None),
            P(None, cols, None),
            P("row", cols, None),
            P("row", cols, None),
        ),
        out_specs=P(("row", "z", "c"), None, None),
        check_vma=False,
    )
```
